256 devices in a mesh: lat: 16 (over z_hi, y, core), lon: 16 (over x, z_lo).
Axes of the slice: x: 4, y: 4, z: 8 (z_hi: 2, z_lo: 4; z = z_hi * 4 + z_lo), core: 2. Of those that a mesh axis runs over, the one named last changes fastest.
Arguments:
- forward_state: float32 [256, 32768], P(None, ('lat', 'lon')), may hold values from -6 to 6
- adjoint_state: float32 [256, 32768], P(None, ('lat', 'lon')), may hold values from -6 to 6
- inc_forward: float32 [4, 256, 32768], P(None, None, ('lat', 'lon')), may hold values from -6 to 6
- inc_adjoint: float32 [4, 256, 32768], P(None, None, ('lat', 'lon')), may hold values from -6 to 6
- bulk_modulus: float32 [32768], P(('lat', 'lon')), may hold values from 0.5 to 2
- inverse_size: float32 [32768], P(('lat', 'lon')), may hold values from 0.7 to 1.4
- face_codes: int32 [4, 32768], P(None, ('lat', 'lon')), may hold values from 0 to 7
- block_map: int32 [32768], P(('lat', 'lon')), may hold values from 0 to 255
- probe_dirs: float32 [4, 256], P(None, ('lat', 'lon')), may hold values from -6 to 6
Outputs:
- new_forward: float32 [4, 256, 32768], P(None, None, ('lat', 'lon'))
- new_adjoint: float32 [4, 256, 32768], P(None, None, ('lat', 'lon'))
- hess_vec: float32 [4, 256], P(None, ('lat', 'lon'))
The draws below stay inside these ranges and needn't reach their ends.
All inputs are finite; a program needn't handle non-finite values.
Results may differ from the reference program's by a relative error of at most 0.00013.
Values sent between devices are 32-bit elements; how exact they have to be, the bound alone decides.
No kernel may reach another device: no remote copies, remote signals or barrier semaphores. Data moves between devices by JAX's collectives and lax.ppermute only.
A program may use at most 64 MiB of HBM per device.

```python
import math
import jax
import jax.numpy as jnp
import numpy as np
from jax import lax

NR = 128
PROBES = 4
NLAT = 16
NLON = 16
NELEM = 32768
NB = 256


def with_ends(entries, key, smallest, top_value):
    spot = [jax.random.randint(jax.random.fold_in(key, axis), (), 0, length) for axis, length in enumerate(entries.shape)]
    main_axis = entries.shape.index(max(entries.shape))
    next_to = spot[:main_axis] + [(spot[main_axis] + 1) % entries.shape[main_axis]] + spot[main_axis + 1:]
    return entries.at[tuple(spot)].set(smallest).at[tuple(next_to)].set(top_value)


def levels(rng, extent, shards, smallest, high):
    loudness, own = 1.0, jax.random.fold_in(rng, 6)
    for axis_at, shards_of in shards:
        heights = jnp.exp(jax.random.uniform(jax.random.fold_in(own, axis_at), (shards_of,), jnp.float32, smallest / len(shards), high / len(shards)))
        loudness = loudness * jnp.repeat(heights, extent[axis_at] // shards_of).reshape([-1 if axis == axis_at else 1 for axis in range(len(extent))])
    return loudness


def gaussian(key, dims, scale, most, cuts=(), kind=jnp.bfloat16):
    gain = levels(key, dims, cuts, -0.22, 0.18) if cuts else 1.0
    entries = jax.random.normal(key, dims, jnp.float32) * scale * gain
    return jnp.minimum(jnp.maximum(entries, -most), most).astype(kind)


def setup_inputs(seed: int = 0) -> dict:
    seeds = jax.random.split(jax.random.key(seed), 10)
    forward_state = gaussian(seeds[0], (256, NELEM), 1.0, 6.0, ((1, 256),), jnp.float32)
    adjoint_state = gaussian(seeds[1], (256, NELEM), 1.0, 6.0, ((1, 256),), jnp.float32)
    inc_forward = gaussian(seeds[2], (PROBES, 256, NELEM), 1.0, 6.0, ((2, 256),), jnp.float32)
    inc_adjoint = gaussian(seeds[3], (PROBES, 256, NELEM), 1.0, 6.0, ((2, 256),), jnp.float32)
    bulk_modulus = jnp.clip(jnp.exp(math.log(2.0) - 1.3862944 * jax.random.uniform(seeds[4], (NELEM,), jnp.float32) ** levels(seeds[4], (NELEM,), ((0, 256),), -0.2, 0.2)), 0.5, 2.0)
    inverse_size = jnp.clip(jnp.exp(math.log(1.4) - 0.6931472 * jax.random.uniform(seeds[5], (NELEM,), jnp.float32) ** levels(seeds[5], (NELEM,), ((0, 256),), -0.2, 0.2)), 0.7, 1.4)
    face_codes = with_ends(jax.random.randint(seeds[6], (4, NELEM), 0, 8), jax.random.fold_in(seeds[6], 1), 0, 7).astype(jnp.int32)
    block_map = with_ends(jax.random.randint(seeds[7], (NELEM,), 0, NB), jax.random.fold_in(seeds[7], 1), 0, NB - 1).astype(jnp.int32)
    probe_dirs = gaussian(seeds[8], (PROBES, NB), 1.0, 6.0, ((1, 256),), jnp.float32)
    return {"forward_state": forward_state, "adjoint_state": adjoint_state, "inc_forward": inc_forward, "inc_adjoint": inc_adjoint, "bulk_modulus": bulk_modulus, "inverse_size": inverse_size, "face_codes": face_codes, "block_map": block_map, "probe_dirs": probe_dirs}


TIME_STEP = 0.05
PENALTY = 1.0
LIFT_FACTOR = 6.0

def node_tables():
    spread = 1.0 / np.sqrt(5.0)
    points = np.array([-1.0, -spread, spread, 1.0])
    weights = np.array([1.0, 5.0, 5.0, 1.0]) / 6.0
    products = np.array([np.prod([points[j] - points[k] for k in range(4) if k != j]) for j in range(4)])
    derivative = np.zeros((4, 4))
    for i in range(4):
        for j in range(4):
            if i != j:
                derivative[i, j] = products[i] / products[j] / (points[i] - points[j])
        derivative[i, i] = np.sum([1.0 / (points[i] - points[k]) for k in range(4) if k != i])
    identity = np.eye(4)
    directional = [np.kron(derivative, np.kron(identity, identity)), np.kron(identity, np.kron(derivative, identity)), np.kron(identity, np.kron(identity, derivative))]
    coupling = np.zeros((256, 256))
    for d in range(3):
        coupling[64 * (d + 1):64 * (d + 2), 0:64] = directional[d].T
        coupling[0:64, 64 * (d + 1):64 * (d + 2)] = directional[d].T
    selects = np.zeros((256, 192))
    for f in range(6):
        d = f // 2
        for u in range(4):
            for v in range(4):
                position = [u, v]
                position.insert(d, 3 * (f % 2))
                node_id = 16 * position[0] + 4 * position[1] + position[2]
                selects[node_id, 32 * f + 4 * u + v] = 1.0
                selects[64 * (d + 1) + node_id, 32 * f + 16 + 4 * u + v] = 1.0
    orient = np.zeros((8, 32), np.int32)
    for q in range(8):
        for u in range(4):
            for v in range(4):
                source_u, source_v = (v, u) if q & 1 else (u, v)
                if q & 2:
                    source_u = 3 - source_u
                if q & 4:
                    source_v = 3 - source_v
                orient[q, 4 * u + v] = 4 * source_u + source_v
                orient[q, 16 + 4 * u + v] = 16 + 4 * source_u + source_v
    quadrature = np.kron(weights, np.kron(weights, weights))
    return (jnp.asarray(coupling, dtype=jnp.float32), jnp.asarray(selects, dtype=jnp.float32), orient, jnp.asarray(quadrature, dtype=jnp.float32))

def volume_rate(states, coupling, bulk_modulus, inverse_size):
    mixed = jnp.einsum('cd,scr->sdr', coupling, states, precision=lax.Precision.HIGHEST)
    channel = lax.broadcasted_iota(jnp.int32, (256, 1), 0)
    factor = jnp.where(channel < 64, -(bulk_modulus * inverse_size)[None, :], -inverse_size[None, :])
    return mixed * factor[None]

def face_term(own_trace, neighbour, bulk_modulus, inverse_size, normal_sign):
    jump_pressure = neighbour[:, :16] - own_trace[:, :16]
    jump_velocity = neighbour[:, 16:] - own_trace[:, 16:]
    modulus = bulk_modulus[None, None, :]
    lift_scale = LIFT_FACTOR * inverse_size[None, None, :]
    on_pressure = lift_scale * (-modulus * normal_sign * 0.5 * jump_velocity + 0.5 * PENALTY * jump_pressure)
    on_velocity = lift_scale * (-normal_sign * 0.5 * jump_pressure + 0.5 * PENALTY * jump_velocity)
    return jnp.concatenate([on_pressure, on_velocity], 1)

def radial_neighbours(rad_minus, rad_plus):
    below_trace = jnp.concatenate([jnp.zeros_like(rad_plus[..., :1]), rad_plus[..., :-1]], -1)
    above_trace = jnp.concatenate([rad_minus[..., 1:], jnp.zeros_like(rad_minus[..., :1])], -1)
    return (below_trace, above_trace)

def heun_step(states, sources, neighbour_fn, bulk_modulus, inverse_size, coupling, selects):

    def rate_of(field_now):
        traces_all = jnp.einsum('ck,scr->skr', selects, field_now, precision=lax.Precision.HIGHEST)
        traces = [traces_all[:, 32 * f:32 * f + 32] for f in range(6)]
        neighbours = neighbour_fn(traces)
        face_rates = jnp.concatenate([face_term(traces[f], neighbours[f], bulk_modulus, inverse_size, 2.0 * (f % 2) - 1.0) for f in range(6)], 1)
        lifted = jnp.einsum('ck,skr->scr', selects, face_rates, precision=lax.Precision.HIGHEST)
        return volume_rate(field_now, coupling, bulk_modulus, inverse_size) + lifted + sources
    first_rate = rate_of(states)
    second_rate = rate_of(states + TIME_STEP * first_rate)
    return states + 0.5 * TIME_STEP * (first_rate + second_rate)

def divergence(field_state, coupling, inverse_size):
    return -inverse_size * jnp.einsum('cn,...cr->...nr', coupling[:, :64], field_state, precision=lax.Precision.HIGHEST)

def pressure_source(perturb, forward_div, adjoint_div):
    source_terms = jnp.concatenate([perturb[:, None, :] * forward_div[None], perturb[:, None, :] * adjoint_div[None]], 0)
    return jnp.concatenate([source_terms, jnp.zeros((source_terms.shape[0], 192, source_terms.shape[2]), jnp.float32)], 1)

def sensitivity(new_forward, new_adjoint, forward_div, adjoint_state, inverse_size, coupling, quadrature):
    new_div = divergence(new_forward, coupling, inverse_size)
    integrand = new_adjoint[:, :64] * forward_div[None] + adjoint_state[None, :64] * new_div
    return jnp.einsum('n,pnr->pr', quadrature, integrand, precision=lax.Precision.HIGHEST) / (64.0 * inverse_size ** 3)

def reorient(neighbour, codes_face, orient):
    node_index = jnp.asarray(orient, dtype=jnp.int32)[codes_face].T
    return jnp.take_along_axis(neighbour, jnp.broadcast_to(node_index[None], neighbour.shape), axis=1)

def reference(forward_state, adjoint_state, inc_forward, inc_adjoint, bulk_modulus, inverse_size, face_codes, block_map, probe_dirs):
    coupling, selects, orient, quadrature = node_tables()
    forward_div = divergence(forward_state, coupling, inverse_size)
    adjoint_div = divergence(adjoint_state, coupling, inverse_size)
    perturb = jnp.take(probe_dirs, block_map, axis=1)

    def neighbour_fn(traces):
        grid = [t.reshape(t.shape[:2] + (NLAT, NLON, NR)) for t in traces]
        from_south = jnp.concatenate([jnp.zeros_like(grid[1][:, :, :1]), grid[1][:, :, :-1]], 2)
        from_north = jnp.concatenate([grid[0][:, :, 1:], jnp.zeros_like(grid[0][:, :, :1])], 2)
        from_west = jnp.roll(grid[3], 1, axis=3)
        from_east = jnp.roll(grid[2], -1, axis=3)
        below_trace, above_trace = radial_neighbours(grid[4], grid[5])
        sides = [from_south, from_north, from_west, from_east, below_trace, above_trace]
        flat = [t.reshape(t.shape[:2] + (NLAT * NLON * NR,)) for t in sides]
        return [reorient(flat[f], face_codes[f], orient) for f in range(4)] + flat[4:]

    def one_probe(probe_items):
        probe_forward, probe_adjoint, probe_perturb = probe_items
        states = jnp.stack([probe_forward, probe_adjoint])
        sources = pressure_source(probe_perturb[None], forward_div, adjoint_div)
        updated = heun_step(states, sources, neighbour_fn, bulk_modulus, inverse_size, coupling, selects)
        return (updated[0], updated[1])
    new_forward, new_adjoint = lax.map(one_probe, (inc_forward, inc_adjoint, perturb))
    element_terms = sensitivity(new_forward, new_adjoint, forward_div, adjoint_state, inverse_size, coupling, quadrature)
    hess_vec = jax.ops.segment_sum(element_terms.T, block_map, num_segments=NB).T
    return (new_forward, new_adjoint, hess_vec)
```

```python
import jax
import jax.numpy as jnp
import numpy as np
from jax import lax
from jax.sharding import PartitionSpec as P

TIME_STEP = 0.05
PENALTY = 1.0
LIFT_FACTOR = 6.0


def shifted(block, axis, distance):
    devices = range(lax.axis_size(axis))
    route = [(i - distance, i) for i in devices if i - distance in devices]
    return lax.ppermute(block, axis, route)


def from_behind(value, axis, steps):
    count = lax.axis_size(axis)
    pairs = [(source, (source + steps) % count) for source in range(count)]
    return lax.ppermute(value, axis, pairs)


def node_tables():
    spread = 1.0 / np.sqrt(5.0)
    points = np.array([-1.0, -spread, spread, 1.0])
    weights = np.array([1.0, 5.0, 5.0, 1.0]) / 6.0
    products = np.array(
        [np.prod([points[j] - points[k] for k in range(4) if k != j]) for j in range(4)]
    )
    derivative = np.zeros((4, 4))
    for i in range(4):
        for j in range(4):
            if i != j:
                derivative[i, j] = products[i] / products[j] / (points[i] - points[j])
        derivative[i, i] = np.sum([1.0 / (points[i] - points[k]) for k in range(4) if k != i])
    identity = np.eye(4)
    directional = [
        np.kron(derivative, np.kron(identity, identity)),
        np.kron(identity, np.kron(derivative, identity)),
        np.kron(identity, np.kron(identity, derivative)),
    ]
    coupling = np.zeros((256, 256))
    for d in range(3):
        coupling[64 * (d + 1) : 64 * (d + 2), 0:64] = directional[d].T
        coupling[0:64, 64 * (d + 1) : 64 * (d + 2)] = directional[d].T
    selects = np.zeros((256, 192))
    for f in range(6):
        d = f // 2
        for u in range(4):
            for v in range(4):
                position = [u, v]
                position.insert(d, 3 * (f % 2))
                node_id = 16 * position[0] + 4 * position[1] + position[2]
                selects[node_id, 32 * f + 4 * u + v] = 1.0
                selects[64 * (d + 1) + node_id, 32 * f + 16 + 4 * u + v] = 1.0
    orient = np.zeros((8, 32), np.int32)
    for q in range(8):
        for u in range(4):
            for v in range(4):
                source_u, source_v = (v, u) if q & 1 else (u, v)
                if q & 2:
                    source_u = 3 - source_u
                if q & 4:
                    source_v = 3 - source_v
                orient[q, 4 * u + v] = 4 * source_u + source_v
                orient[q, 16 + 4 * u + v] = 16 + 4 * source_u + source_v
    quadrature = np.kron(weights, np.kron(weights, weights))
    return (
        jnp.asarray(coupling, dtype=jnp.float32),
        jnp.asarray(selects, dtype=jnp.float32),
        orient,
        jnp.asarray(quadrature, dtype=jnp.float32),
    )


def volume_rate(states, coupling, bulk_modulus, inverse_size):
    mixed = jnp.einsum("cd,scr->sdr", coupling, states, precision=lax.Precision.HIGHEST)
    channel = lax.broadcasted_iota(jnp.int32, (256, 1), 0)
    factor = jnp.where(
        channel < 64, -(bulk_modulus * inverse_size)[None, :], -inverse_size[None, :]
    )
    return mixed * factor[None]


def face_term(own_trace, neighbour, bulk_modulus, inverse_size, normal_sign):
    jump_pressure = neighbour[:, :16] - own_trace[:, :16]
    jump_velocity = neighbour[:, 16:] - own_trace[:, 16:]
    modulus = bulk_modulus[None, None, :]
    lift_scale = LIFT_FACTOR * inverse_size[None, None, :]
    on_pressure = lift_scale * (
        -modulus * normal_sign * 0.5 * jump_velocity + 0.5 * PENALTY * jump_pressure
    )
    on_velocity = lift_scale * (-normal_sign * 0.5 * jump_pressure + 0.5 * PENALTY * jump_velocity)
    return jnp.concatenate([on_pressure, on_velocity], 1)


def radial_neighbours(rad_minus, rad_plus):
    below_trace = jnp.concatenate([jnp.zeros_like(rad_plus[..., :1]), rad_plus[..., :-1]], -1)
    above_trace = jnp.concatenate([rad_minus[..., 1:], jnp.zeros_like(rad_minus[..., :1])], -1)
    return (below_trace, above_trace)


def heun_step(states, sources, neighbour_fn, bulk_modulus, inverse_size, coupling, selects):

    def rate_of(field_now):
        traces_all = jnp.einsum("ck,scr->skr", selects, field_now, precision=lax.Precision.HIGHEST)
        traces = [traces_all[:, 32 * f : 32 * f + 32] for f in range(6)]
        neighbours = neighbour_fn(traces)
        face_rates = jnp.concatenate(
            [
                face_term(traces[f], neighbours[f], bulk_modulus, inverse_size, 2.0 * (f % 2) - 1.0)
                for f in range(6)
            ],
            1,
        )
        lifted = jnp.einsum("ck,skr->scr", selects, face_rates, precision=lax.Precision.HIGHEST)
        return volume_rate(field_now, coupling, bulk_modulus, inverse_size) + lifted + sources

    first_rate = rate_of(states)
    second_rate = rate_of(states + TIME_STEP * first_rate)
    return states + 0.5 * TIME_STEP * (first_rate + second_rate)


def divergence(field_state, coupling, inverse_size):
    return -inverse_size * jnp.einsum(
        "cn,...cr->...nr", coupling[:, :64], field_state, precision=lax.Precision.HIGHEST
    )


def pressure_source(perturb, forward_div, adjoint_div):
    source_terms = jnp.concatenate(
        [perturb[:, None, :] * forward_div[None], perturb[:, None, :] * adjoint_div[None]], 0
    )
    return jnp.concatenate(
        [source_terms, jnp.zeros((source_terms.shape[0], 192, source_terms.shape[2]), jnp.float32)],
        1,
    )


def sensitivity(
    new_forward, new_adjoint, forward_div, adjoint_state, inverse_size, coupling, quadrature
):
    new_div = divergence(new_forward, coupling, inverse_size)
    integrand = new_adjoint[:, :64] * forward_div[None] + adjoint_state[None, :64] * new_div
    return jnp.einsum("n,pnr->pr", quadrature, integrand, precision=lax.Precision.HIGHEST) / (
        64.0 * inverse_size**3
    )


def reorient(neighbour, codes_face, orient):
    states, channels, count = neighbour.shape
    grid = neighbour.reshape(states, channels // 16, 4, 4, count)
    bits = [(codes_face & (1 << b)) != 0 for b in range(3)]
    flipped_v = jnp.flip(grid, 3)
    grid = jnp.where(bits[2][None, None, None, None, :], flipped_v, grid)
    flipped_u = jnp.flip(grid, 2)
    grid = jnp.where(bits[1][None, None, None, None, :], flipped_u, grid)
    swapped = jnp.swapaxes(grid, 2, 3)
    grid = jnp.where(bits[0][None, None, None, None, :], swapped, grid)
    return grid.reshape(states, channels, count)


def gather_blocks(block):
    for axis in ("lon", "lat"):
        size = lax.axis_size(axis)
        me = lax.axis_index(axis)
        step = 1
        while step < size:
            pairs = [(i, i ^ step) for i in range(size)]
            other = lax.ppermute(block, axis, pairs)
            upper = ((me // step) % 2) == 1
            block = jnp.where(upper, jnp.concatenate([other, block], -1),
                              jnp.concatenate([block, other], -1))
            step *= 2
    return block


def scatter_sums(partial):
    for axis in ("lat", "lon"):
        size = lax.axis_size(axis)
        me = lax.axis_index(axis)
        step = size // 2
        while step >= 1:
            half = partial.shape[-1] // 2
            low, high = partial[..., :half], partial[..., half:]
            upper = ((me // step) % 2) == 1
            keep = jnp.where(upper, high, low)
            give = jnp.where(upper, low, high)
            pairs = [(i, i ^ step) for i in range(size)]
            partial = keep + lax.ppermute(give, axis, pairs)
            step //= 2
    return partial


def shift_lat(rim, offset):
    return shifted(rim, "lat", offset)


def shift_lon(rim, offset):
    return from_behind(rim, "lon", offset)


def rims_lat(first_rim, last_rim):
    from_south = shift_lat(last_rim, 1)
    from_north = shift_lat(first_rim, -1)
    return (from_south, from_north)


def rims_lon(first_rim, last_rim):
    from_west = shift_lon(last_rim, 1)
    from_east = shift_lon(first_rim, -1)
    return (from_west, from_east)


def body(
    forward_state,
    adjoint_state,
    inc_forward,
    inc_adjoint,
    bulk_modulus,
    inverse_size,
    face_codes,
    block_map,
    probe_dirs,
):
    coupling, selects, orient, quadrature = node_tables()
    whole_dirs = gather_blocks(probe_dirs)
    perturb = jnp.take(whole_dirs, block_map, axis=1)
    forward_div = divergence(forward_state, coupling, inverse_size)
    adjoint_div = divergence(adjoint_state, coupling, inverse_size)

    def neighbour_fn(traces):
        from_south, from_north = rims_lat(traces[0], traces[1])
        from_west, from_east = rims_lon(traces[2], traces[3])
        sides = [from_south, from_north, from_west, from_east]
        horizontal = [reorient(sides[f], face_codes[f], orient) for f in range(4)]
        below_trace, above_trace = radial_neighbours(traces[4], traces[5])
        return horizontal + [below_trace, above_trace]

    probe_count = inc_forward.shape[0]
    states = jnp.concatenate([inc_forward, inc_adjoint], 0)
    sources = pressure_source(perturb, forward_div, adjoint_div)
    updated = heun_step(
        states, sources, neighbour_fn, bulk_modulus, inverse_size, coupling, selects
    )
    new_forward = updated[:probe_count]
    new_adjoint = updated[probe_count:]
    element_terms = sensitivity(
        new_forward, new_adjoint, forward_div, adjoint_state, inverse_size, coupling, quadrature
    )
    partial_sums = jax.ops.segment_sum(
        element_terms.T, block_map, num_segments=whole_dirs.shape[1]
    ).T
    hess_vec = scatter_sums(partial_sums)
    return (new_forward, new_adjoint, hess_vec)


def solution(mesh):
    placed = (
        P(None, ("lat", "lon")),
        P(None, ("lat", "lon")),
        P(None, None, ("lat", "lon")),
        P(None, None, ("lat", "lon")),
        P(("lat", "lon")),
        P(("lat", "lon")),
        P(None, ("lat", "lon")),
        P(("lat", "lon")),
        P(None, ("lat", "lon")),
    )
    return jax.shard_map(
        body,
        mesh=mesh,
        in_specs=placed,
        out_specs=(
            P(None, None, ("lat", "lon")),
            P(None, None, ("lat", "lon")),
            P(None, ("lat", "lon")),
        ),
        check_vma=False,
    )
```

```python
import jax
import jax.numpy as jnp
import numpy as np
from jax import lax
from jax.sharding import PartitionSpec as P

TIME_STEP = 0.05
PENALTY = 1.0
LIFT_FACTOR = 6.0


def shifted(block, axis, distance):
    devices = range(lax.axis_size(axis))
    route = [(i - distance, i) for i in devices if i - distance in devices]
    return lax.ppermute(block, axis, route)


def from_behind(value, axis, steps):
    count = lax.axis_size(axis)
    pairs = [(source, (source + steps) % count) for source in range(count)]
    return lax.ppermute(value, axis, pairs)


def node_tables():
    spread = 1.0 / np.sqrt(5.0)
    points = np.array([-1.0, -spread, spread, 1.0])
    weights = np.array([1.0, 5.0, 5.0, 1.0]) / 6.0
    products = np.array(
        [np.prod([points[j] - points[k] for k in range(4) if k != j]) for j in range(4)]
    )
    derivative = np.zeros((4, 4))
    for i in range(4):
        for j in range(4):
            if i != j:
                derivative[i, j] = products[i] / products[j] / (points[i] - points[j])
        derivative[i, i] = np.sum([1.0 / (points[i] - points[k]) for k in range(4) if k != i])
    identity = np.eye(4)
    directional = [
        np.kron(derivative, np.kron(identity, identity)),
        np.kron(identity, np.kron(derivative, identity)),
        np.kron(identity, np.kron(identity, derivative)),
    ]
    coupling = np.zeros((256, 256))
    for d in range(3):
        coupling[64 * (d + 1) : 64 * (d + 2), 0:64] = directional[d].T
        coupling[0:64, 64 * (d + 1) : 64 * (d + 2)] = directional[d].T
    selects = np.zeros((256, 192))
    for f in range(6):
        d = f // 2
        for u in range(4):
            for v in range(4):
                position = [u, v]
                position.insert(d, 3 * (f % 2))
                node_id = 16 * position[0] + 4 * position[1] + position[2]
                selects[node_id, 32 * f + 4 * u + v] = 1.0
                selects[64 * (d + 1) + node_id, 32 * f + 16 + 4 * u + v] = 1.0
    orient = np.zeros((8, 32), np.int32)
    for q in range(8):
        for u in range(4):
            for v in range(4):
                source_u, source_v = (v, u) if q & 1 else (u, v)
                if q & 2:
                    source_u = 3 - source_u
                if q & 4:
                    source_v = 3 - source_v
                orient[q, 4 * u + v] = 4 * source_u + source_v
                orient[q, 16 + 4 * u + v] = 16 + 4 * source_u + source_v
    quadrature = np.kron(weights, np.kron(weights, weights))
    return (
        jnp.asarray(coupling, dtype=jnp.float32),
        jnp.asarray(selects, dtype=jnp.float32),
        orient,
        jnp.asarray(quadrature, dtype=jnp.float32),
    )


def volume_rate(states, coupling, bulk_modulus, inverse_size):
    mixed = jnp.einsum("cd,scr->sdr", coupling, states, precision=lax.Precision.HIGHEST)
    channel = lax.broadcasted_iota(jnp.int32, (256, 1), 0)
    factor = jnp.where(
        channel < 64, -(bulk_modulus * inverse_size)[None, :], -inverse_size[None, :]
    )
    return mixed * factor[None]


def face_term(own_trace, neighbour, bulk_modulus, inverse_size, normal_sign):
    jump_pressure = neighbour[:, :16] - own_trace[:, :16]
    jump_velocity = neighbour[:, 16:] - own_trace[:, 16:]
    modulus = bulk_modulus[None, None, :]
    lift_scale = LIFT_FACTOR * inverse_size[None, None, :]
    on_pressure = lift_scale * (
        -modulus * normal_sign * 0.5 * jump_velocity + 0.5 * PENALTY * jump_pressure
    )
    on_velocity = lift_scale * (-normal_sign * 0.5 * jump_pressure + 0.5 * PENALTY * jump_velocity)
    return jnp.concatenate([on_pressure, on_velocity], 1)


def radial_neighbours(rad_minus, rad_plus):
    below_trace = jnp.concatenate([jnp.zeros_like(rad_plus[..., :1]), rad_plus[..., :-1]], -1)
    above_trace = jnp.concatenate([rad_minus[..., 1:], jnp.zeros_like(rad_minus[..., :1])], -1)
    return (below_trace, above_trace)


def heun_step(states, sources, neighbour_fn, bulk_modulus, inverse_size, coupling, selects):

    def rate_of(field_now):
        traces_all = jnp.einsum("ck,scr->skr", selects, field_now, precision=lax.Precision.HIGHEST)
        traces = [traces_all[:, 32 * f : 32 * f + 32] for f in range(6)]
        neighbours = neighbour_fn(traces)
        face_rates = jnp.concatenate(
            [
                face_term(traces[f], neighbours[f], bulk_modulus, inverse_size, 2.0 * (f % 2) - 1.0)
                for f in range(6)
            ],
            1,
        )
        lifted = jnp.einsum("ck,skr->scr", selects, face_rates, precision=lax.Precision.HIGHEST)
        return volume_rate(field_now, coupling, bulk_modulus, inverse_size) + lifted + sources

    first_rate = rate_of(states)
    second_rate = rate_of(states + TIME_STEP * first_rate)
    return states + 0.5 * TIME_STEP * (first_rate + second_rate)


def divergence(field_state, coupling, inverse_size):
    return -inverse_size * jnp.einsum(
        "cn,...cr->...nr", coupling[:, :64], field_state, precision=lax.Precision.HIGHEST
    )


def pressure_source(perturb, forward_div, adjoint_div):
    source_terms = jnp.concatenate(
        [perturb[:, None, :] * forward_div[None], perturb[:, None, :] * adjoint_div[None]], 0
    )
    return jnp.concatenate(
        [source_terms, jnp.zeros((source_terms.shape[0], 192, source_terms.shape[2]), jnp.float32)],
        1,
    )


def sensitivity(
    new_forward, new_adjoint, forward_div, adjoint_state, inverse_size, coupling, quadrature
):
    new_div = divergence(new_forward, coupling, inverse_size)
    integrand = new_adjoint[:, :64] * forward_div[None] + adjoint_state[None, :64] * new_div
    return jnp.einsum("n,pnr->pr", quadrature, integrand, precision=lax.Precision.HIGHEST) / (
        64.0 * inverse_size**3
    )


def reorient(neighbour, codes_face, orient):
    choices = np.zeros((orient.shape[0], 32, 32), np.float32)
    for code in range(orient.shape[0]):
        choices[code, np.arange(32), orient[code]] = 1.0
    candidates = jnp.einsum(
        "qkj,sjr->qskr", jnp.asarray(choices), neighbour, precision=lax.Precision.HIGHEST
    )
    result = candidates[0]
    for code in range(1, orient.shape[0]):
        result = jnp.where((codes_face == code)[None, None, :], candidates[code], result)
    return result


def gather_blocks(block):
    count = lax.axis_size(("lat", "lon"))
    spread = jnp.broadcast_to(block.T, (count, block.shape[0]))
    return lax.all_to_all(spread, ("lat", "lon"), 0, 0, tiled=True).T


def scatter_sums(partial):
    pieces = lax.all_to_all(partial.T, ("lat", "lon"), 0, 0, tiled=True)
    return jnp.sum(pieces, 0)[:, None]


def shift_lat(rim, offset):
    return shifted(rim, "lat", offset)


def shift_lon(rim, offset):
    return from_behind(rim, "lon", offset)


def rims_lat(first_rim, last_rim):
    from_south = shift_lat(last_rim, 1)
    from_north = shift_lat(first_rim, -1)
    return (from_south, from_north)


def rims_lon(first_rim, last_rim):
    from_west = shift_lon(last_rim, 1)
    from_east = shift_lon(first_rim, -1)
    return (from_west, from_east)


def body(
    forward_state,
    adjoint_state,
    inc_forward,
    inc_adjoint,
    bulk_modulus,
    inverse_size,
    face_codes,
    block_map,
    probe_dirs,
):
    coupling, selects, orient, quadrature = node_tables()
    whole_dirs = gather_blocks(probe_dirs)
    perturb = jnp.take(whole_dirs, block_map, axis=1)
    forward_div = divergence(forward_state, coupling, inverse_size)
    adjoint_div = divergence(adjoint_state, coupling, inverse_size)

    def neighbour_fn(traces):
        from_south, from_north = rims_lat(traces[0], traces[1])
        from_west, from_east = rims_lon(traces[2], traces[3])
        sides = [from_south, from_north, from_west, from_east]
        horizontal = [reorient(sides[f], face_codes[f], orient) for f in range(4)]
        below_trace, above_trace = radial_neighbours(traces[4], traces[5])
        return horizontal + [below_trace, above_trace]

    probe_count = inc_forward.shape[0]
    states = jnp.concatenate([inc_forward, inc_adjoint], 0)
    sources = pressure_source(perturb, forward_div, adjoint_div)
    updated = heun_step(
        states, sources, neighbour_fn, bulk_modulus, inverse_size, coupling, selects
    )
    new_forward = updated[:probe_count]
    new_adjoint = updated[probe_count:]
    element_terms = sensitivity(
        new_forward, new_adjoint, forward_div, adjoint_state, inverse_size, coupling, quadrature
    )
    partial_sums = jax.ops.segment_sum(
        element_terms.T, block_map, num_segments=whole_dirs.shape[1]
    ).T
    hess_vec = scatter_sums(partial_sums)
    return (new_forward, new_adjoint, hess_vec)


def solution(mesh):
    placed = (
        P(None, ("lat", "lon")),
        P(None, ("lat", "lon")),
        P(None, None, ("lat", "lon")),
        P(None, None, ("lat", "lon")),
        P(("lat", "lon")),
        P(("lat", "lon")),
        P(None, ("lat", "lon")),
        P(("lat", "lon")),
        P(None, ("lat", "lon")),
    )
    return jax.shard_map(
        body,
        mesh=mesh,
        in_specs=placed,
        out_specs=(
            P(None, None, ("lat", "lon")),
            P(None, None, ("lat", "lon")),
            P(None, ("lat", "lon")),
        ),
        check_vma=False,
    )
```

```python
import jax
import jax.numpy as jnp
import numpy as np
from jax import lax
from jax.sharding import PartitionSpec as P

TIME_STEP = 0.05
PENALTY = 1.0
LIFT_FACTOR = 6.0


def shifted(block, axis, distance):
    devices = range(lax.axis_size(axis))
    route = [(i - distance, i) for i in devices if i - distance in devices]
    return lax.ppermute(block, axis, route)


def from_behind(value, axis, steps):
    count = lax.axis_size(axis)
    pairs = [(source, (source + steps) % count) for source in range(count)]
    return lax.ppermute(value, axis, pairs)


def node_tables():
    spread = 1.0 / np.sqrt(5.0)
    points = np.array([-1.0, -spread, spread, 1.0])
    weights = np.array([1.0, 5.0, 5.0, 1.0]) / 6.0
    products = np.array(
        [np.prod([points[j] - points[k] for k in range(4) if k != j]) for j in range(4)]
    )
    derivative = np.zeros((4, 4))
    for i in range(4):
        for j in range(4):
            if i != j:
                derivative[i, j] = products[i] / products[j] / (points[i] - points[j])
        derivative[i, i] = np.sum([1.0 / (points[i] - points[k]) for k in range(4) if k != i])
    identity = np.eye(4)
    directional = [
        np.kron(derivative, np.kron(identity, identity)),
        np.kron(identity, np.kron(derivative, identity)),
        np.kron(identity, np.kron(identity, derivative)),
    ]
    coupling = np.zeros((256, 256))
    for d in range(3):
        coupling[64 * (d + 1) : 64 * (d + 2), 0:64] = directional[d].T
        coupling[0:64, 64 * (d + 1) : 64 * (d + 2)] = directional[d].T
    selects = np.zeros((256, 192))
    for f in range(6):
        d = f // 2
        for u in range(4):
            for v in range(4):
                position = [u, v]
                position.insert(d, 3 * (f % 2))
                node_id = 16 * position[0] + 4 * position[1] + position[2]
                selects[node_id, 32 * f + 4 * u + v] = 1.0
                selects[64 * (d + 1) + node_id, 32 * f + 16 + 4 * u + v] = 1.0
    orient = np.zeros((8, 32), np.int32)
    for q in range(8):
        for u in range(4):
            for v in range(4):
                source_u, source_v = (v, u) if q & 1 else (u, v)
                if q & 2:
                    source_u = 3 - source_u
                if q & 4:
                    source_v = 3 - source_v
                orient[q, 4 * u + v] = 4 * source_u + source_v
                orient[q, 16 + 4 * u + v] = 16 + 4 * source_u + source_v
    quadrature = np.kron(weights, np.kron(weights, weights))
    return (
        jnp.asarray(coupling, dtype=jnp.float32),
        jnp.asarray(selects, dtype=jnp.float32),
        orient,
        jnp.asarray(quadrature, dtype=jnp.float32),
    )


def volume_rate(states, coupling, bulk_modulus, inverse_size):
    mixed = jnp.einsum("cd,scr->sdr", coupling, states, precision=lax.Precision.HIGHEST)
    channel = lax.broadcasted_iota(jnp.int32, (256, 1), 0)
    factor = jnp.where(
        channel < 64, -(bulk_modulus * inverse_size)[None, :], -inverse_size[None, :]
    )
    return mixed * factor[None]


def face_term(own_trace, neighbour, bulk_modulus, inverse_size, normal_sign):
    jump_pressure = neighbour[:, :16] - own_trace[:, :16]
    jump_velocity = neighbour[:, 16:] - own_trace[:, 16:]
    modulus = bulk_modulus[None, None, :]
    lift_scale = LIFT_FACTOR * inverse_size[None, None, :]
    on_pressure = lift_scale * (
        -modulus * normal_sign * 0.5 * jump_velocity + 0.5 * PENALTY * jump_pressure
    )
    on_velocity = lift_scale * (-normal_sign * 0.5 * jump_pressure + 0.5 * PENALTY * jump_velocity)
    return jnp.concatenate([on_pressure, on_velocity], 1)


def radial_neighbours(rad_minus, rad_plus):
    below_trace = jnp.concatenate([jnp.zeros_like(rad_plus[..., :1]), rad_plus[..., :-1]], -1)
    above_trace = jnp.concatenate([rad_minus[..., 1:], jnp.zeros_like(rad_minus[..., :1])], -1)
    return (below_trace, above_trace)


def heun_step(states, sources, neighbour_fn, bulk_modulus, inverse_size, coupling, selects):

    def rate_of(field_now):
        traces_all = jnp.einsum("ck,scr->skr", selects, field_now, precision=lax.Precision.HIGHEST)
        traces = [traces_all[:, 32 * f : 32 * f + 32] for f in range(6)]
        neighbours = neighbour_fn(traces)
        face_rates = jnp.concatenate(
            [
                face_term(traces[f], neighbours[f], bulk_modulus, inverse_size, 2.0 * (f % 2) - 1.0)
                for f in range(6)
            ],
            1,
        )
        lifted = jnp.einsum("ck,skr->scr", selects, face_rates, precision=lax.Precision.HIGHEST)
        return volume_rate(field_now, coupling, bulk_modulus, inverse_size) + lifted + sources

    first_rate = rate_of(states)
    second_rate = rate_of(states + TIME_STEP * first_rate)
    return states + 0.5 * TIME_STEP * (first_rate + second_rate)


def divergence(field_state, coupling, inverse_size):
    return -inverse_size * jnp.einsum(
        "cn,...cr->...nr", coupling[:, :64], field_state, precision=lax.Precision.HIGHEST
    )


def pressure_source(perturb, forward_div, adjoint_div):
    source_terms = jnp.concatenate(
        [perturb[:, None, :] * forward_div[None], perturb[:, None, :] * adjoint_div[None]], 0
    )
    return jnp.concatenate(
        [source_terms, jnp.zeros((source_terms.shape[0], 192, source_terms.shape[2]), jnp.float32)],
        1,
    )


def sensitivity(
    new_forward, new_adjoint, forward_div, adjoint_state, inverse_size, coupling, quadrature
):
    new_div = divergence(new_forward, coupling, inverse_size)
    integrand = new_adjoint[:, :64] * forward_div[None] + adjoint_state[None, :64] * new_div
    return jnp.einsum("n,pnr->pr", quadrature, integrand, precision=lax.Precision.HIGHEST) / (
        64.0 * inverse_size**3
    )


def reorient(sides, codes, orient):
    choices = np.zeros((orient.shape[0], 32, 32), np.float32)
    for code in range(orient.shape[0]):
        choices[code, np.arange(32), orient[code]] = 1.0
    candidates = jnp.einsum(
        "qkj,fsjr->qfskr", jnp.asarray(choices), jnp.stack(sides, 0),
        precision=lax.Precision.HIGHEST,
    )
    result = candidates[0]
    for code in range(1, orient.shape[0]):
        result = jnp.where((codes == code)[:, None, None, :], candidates[code], result)
    return [result[f] for f in range(len(sides))]


def gather_blocks(block):
    count = lax.axis_size(("lat", "lon"))
    spread = jnp.broadcast_to(block.T, (count, block.shape[0]))
    return lax.all_to_all(spread, ("lat", "lon"), 0, 0, tiled=True).T


def scatter_sums(partial):
    pieces = lax.all_to_all(partial.T, ("lat", "lon"), 0, 0, tiled=True)
    return jnp.sum(pieces, 0)[:, None]


def shift_lat(rim, offset):
    return shifted(rim, "lat", offset)


def shift_lon(rim, offset):
    return from_behind(rim, "lon", offset)


def rims_lat(first_rim, last_rim):
    from_south = shift_lat(last_rim, 1)
    from_north = shift_lat(first_rim, -1)
    return (from_south, from_north)


def rims_lon(first_rim, last_rim):
    from_west = shift_lon(last_rim, 1)
    from_east = shift_lon(first_rim, -1)
    return (from_west, from_east)


def body(
    forward_state,
    adjoint_state,
    inc_forward,
    inc_adjoint,
    bulk_modulus,
    inverse_size,
    face_codes,
    block_map,
    probe_dirs,
):
    coupling, selects, orient, quadrature = node_tables()
    whole_dirs = gather_blocks(probe_dirs)
    owners = block_map[None, :] == jnp.arange(whole_dirs.shape[1])[:, None]
    perturb = jnp.einsum(
        "qb,be->qe", whole_dirs, owners.astype(jnp.float32), precision=lax.Precision.HIGHEST
    )
    forward_div = divergence(forward_state, coupling, inverse_size)
    adjoint_div = divergence(adjoint_state, coupling, inverse_size)

    def neighbour_fn(traces):
        from_south, from_north = rims_lat(traces[0], traces[1])
        from_west, from_east = rims_lon(traces[2], traces[3])
        sides = [from_south, from_north, from_west, from_east]
        horizontal = reorient(sides, face_codes, orient)
        below_trace, above_trace = radial_neighbours(traces[4], traces[5])
        return horizontal + [below_trace, above_trace]

    probe_count = inc_forward.shape[0]
    states = jnp.concatenate([inc_forward, inc_adjoint], 0)
    sources = pressure_source(perturb, forward_div, adjoint_div)
    updated = heun_step(
        states, sources, neighbour_fn, bulk_modulus, inverse_size, coupling, selects
    )
    new_forward = updated[:probe_count]
    new_adjoint = updated[probe_count:]
    element_terms = sensitivity(
        new_forward, new_adjoint, forward_div, adjoint_state, inverse_size, coupling, quadrature
    )
    partial_sums = jax.ops.segment_sum(
        element_terms.T, block_map, num_segments=whole_dirs.shape[1]
    ).T
    hess_vec = scatter_sums(partial_sums)
    return (new_forward, new_adjoint, hess_vec)


def solution(mesh):
    placed = (
        P(None, ("lat", "lon")),
        P(None, ("lat", "lon")),
        P(None, None, ("lat", "lon")),
        P(None, None, ("lat", "lon")),
        P(("lat", "lon")),
        P(("lat", "lon")),
        P(None, ("lat", "lon")),
        P(("lat", "lon")),
        P(None, ("lat", "lon")),
    )
    return jax.shard_map(
        body,
        mesh=mesh,
        in_specs=placed,
        out_specs=(
            P(None, None, ("lat", "lon")),
            P(None, None, ("lat", "lon")),
            P(None, ("lat", "lon")),
        ),
        check_vma=False,
    )
```

```python
import jax
import jax.numpy as jnp
import numpy as np
from jax import lax
from jax.sharding import PartitionSpec as P

TIME_STEP = 0.05
PENALTY = 1.0
LIFT_FACTOR = 6.0


def shifted(block, axis, distance):
    devices = range(lax.axis_size(axis))
    route = [(i - distance, i) for i in devices if i - distance in devices]
    return lax.ppermute(block, axis, route)


def from_behind(value, axis, steps):
    count = lax.axis_size(axis)
    pairs = [(source, (source + steps) % count) for source in range(count)]
    return lax.ppermute(value, axis, pairs)


def node_tables():
    spread = 1.0 / np.sqrt(5.0)
    points = np.array([-1.0, -spread, spread, 1.0])
    weights = np.array([1.0, 5.0, 5.0, 1.0]) / 6.0
    products = np.array(
        [np.prod([points[j] - points[k] for k in range(4) if k != j]) for j in range(4)]
    )
    derivative = np.zeros((4, 4))
    for i in range(4):
        for j in range(4):
            if i != j:
                derivative[i, j] = products[i] / products[j] / (points[i] - points[j])
        derivative[i, i] = np.sum([1.0 / (points[i] - points[k]) for k in range(4) if k != i])
    identity = np.eye(4)
    directional = [
        np.kron(derivative, np.kron(identity, identity)),
        np.kron(identity, np.kron(derivative, identity)),
        np.kron(identity, np.kron(identity, derivative)),
    ]
    coupling = np.zeros((256, 256))
    for d in range(3):
        coupling[64 * (d + 1) : 64 * (d + 2), 0:64] = directional[d].T
        coupling[0:64, 64 * (d + 1) : 64 * (d + 2)] = directional[d].T
    selects = np.zeros((256, 192))
    for f in range(6):
        d = f // 2
        for u in range(4):
            for v in range(4):
                position = [u, v]
                position.insert(d, 3 * (f % 2))
                node_id = 16 * position[0] + 4 * position[1] + position[2]
                selects[node_id, 32 * f + 4 * u + v] = 1.0
                selects[64 * (d + 1) + node_id, 32 * f + 16 + 4 * u + v] = 1.0
    orient = np.zeros((8, 32), np.int32)
    for q in range(8):
        for u in range(4):
            for v in range(4):
                source_u, source_v = (v, u) if q & 1 else (u, v)
                if q & 2:
                    source_u = 3 - source_u
                if q & 4:
                    source_v = 3 - source_v
                orient[q, 4 * u + v] = 4 * source_u + source_v
                orient[q, 16 + 4 * u + v] = 16 + 4 * source_u + source_v
    quadrature = np.kron(weights, np.kron(weights, weights))
    return (
        jnp.asarray(coupling, dtype=jnp.float32),
        jnp.asarray(selects, dtype=jnp.float32),
        orient,
        jnp.asarray(quadrature, dtype=jnp.float32),
    )


def volume_rate(states, coupling, bulk_modulus, inverse_size):
    mixed = jnp.einsum("cd,scr->sdr", coupling, states, precision=lax.Precision.HIGHEST)
    channel = lax.broadcasted_iota(jnp.int32, (256, 1), 0)
    factor = jnp.where(
        channel < 64, -(bulk_modulus * inverse_size)[None, :], -inverse_size[None, :]
    )
    return mixed * factor[None]


def face_term(own_trace, neighbour, bulk_modulus, inverse_size, normal_sign):
    jump_pressure = neighbour[:, :16] - own_trace[:, :16]
    jump_velocity = neighbour[:, 16:] - own_trace[:, 16:]
    modulus = bulk_modulus[None, None, :]
    lift_scale = LIFT_FACTOR * inverse_size[None, None, :]
    on_pressure = lift_scale * (
        -modulus * normal_sign * 0.5 * jump_velocity + 0.5 * PENALTY * jump_pressure
    )
    on_velocity = lift_scale * (-normal_sign * 0.5 * jump_pressure + 0.5 * PENALTY * jump_velocity)
    return jnp.concatenate([on_pressure, on_velocity], 1)


def radial_neighbours(rad_minus, rad_plus):
    below_trace = jnp.concatenate([jnp.zeros_like(rad_plus[..., :1]), rad_plus[..., :-1]], -1)
    above_trace = jnp.concatenate([rad_minus[..., 1:], jnp.zeros_like(rad_minus[..., :1])], -1)
    return (below_trace, above_trace)


def heun_step(states, sources, neighbour_fn, bulk_modulus, inverse_size, coupling, selects):

    def rate_of(field_now):
        traces_all = jnp.einsum("ck,scr->skr", selects, field_now, precision=lax.Precision.HIGHEST)
        traces = [traces_all[:, 32 * f : 32 * f + 32] for f in range(6)]
        neighbours = neighbour_fn(traces)
        face_rates = jnp.concatenate(
            [
                face_term(traces[f], neighbours[f], bulk_modulus, inverse_size, 2.0 * (f % 2) - 1.0)
                for f in range(6)
            ],
            1,
        )
        lifted = jnp.einsum("ck,skr->scr", selects, face_rates, precision=lax.Precision.HIGHEST)
        return volume_rate(field_now, coupling, bulk_modulus, inverse_size) + lifted + sources

    first_rate = rate_of(states)
    second_rate = rate_of(states + TIME_STEP * first_rate)
    return states + 0.5 * TIME_STEP * (first_rate + second_rate)


def divergence(field_state, coupling, inverse_size):
    return -inverse_size * jnp.einsum(
        "cn,...cr->...nr", coupling[:, :64], field_state, precision=lax.Precision.HIGHEST
    )


def pressure_source(perturb, forward_div, adjoint_div):
    source_terms = jnp.concatenate(
        [perturb[:, None, :] * forward_div[None], perturb[:, None, :] * adjoint_div[None]], 0
    )
    return jnp.concatenate(
        [source_terms, jnp.zeros((source_terms.shape[0], 192, source_terms.shape[2]), jnp.float32)],
        1,
    )


def sensitivity(
    new_forward, new_adjoint, forward_div, adjoint_state, inverse_size, coupling, quadrature
):
    new_div = divergence(new_forward, coupling, inverse_size)
    integrand = new_adjoint[:, :64] * forward_div[None] + adjoint_state[None, :64] * new_div
    return jnp.einsum("n,pnr->pr", quadrature, integrand, precision=lax.Precision.HIGHEST) / (
        64.0 * inverse_size**3
    )


def face_map(kind):
    picks = np.zeros((32, 32), np.float32)
    for part in range(2):
        for u in range(4):
            for v in range(4):
                su, sv = {"v": (u, 3 - v), "u": (3 - u, v), "t": (v, u)}[kind]
                picks[16 * part + 4 * u + v, 16 * part + 4 * su + sv] = 1.0
    return jnp.asarray(picks)


def reorient(sides, codes, orient):
    stacked = jnp.stack(sides, 0)
    for bit, kind in ((2, "v"), (1, "u"), (0, "t")):
        moved = jnp.einsum(
            "kj,fsjr->fskr", face_map(kind), stacked, precision=lax.Precision.HIGHEST
        )
        stacked = jnp.where(((codes & (1 << bit)) != 0)[:, None, None, :], moved, stacked)
    return [stacked[f] for f in range(len(sides))]


def gather_blocks(block):
    count = lax.axis_size(("lat", "lon"))
    spread = jnp.broadcast_to(block.T, (count, block.shape[0]))
    return lax.all_to_all(spread, ("lat", "lon"), 0, 0, tiled=True).T


def scatter_sums(partial):
    pieces = lax.all_to_all(partial.T, ("lat", "lon"), 0, 0, tiled=True)
    return jnp.sum(pieces, 0)[:, None]


def shift_lat(rim, offset):
    return shifted(rim, "lat", offset)


def shift_lon(rim, offset):
    return from_behind(rim, "lon", offset)


def rims_lat(first_rim, last_rim):
    from_south = shift_lat(last_rim, 1)
    from_north = shift_lat(first_rim, -1)
    return (from_south, from_north)


def rims_lon(first_rim, last_rim):
    from_west = shift_lon(last_rim, 1)
    from_east = shift_lon(first_rim, -1)
    return (from_west, from_east)


def body(
    forward_state,
    adjoint_state,
    inc_forward,
    inc_adjoint,
    bulk_modulus,
    inverse_size,
    face_codes,
    block_map,
    probe_dirs,
):
    coupling, selects, orient, quadrature = node_tables()
    whole_dirs = gather_blocks(probe_dirs)
    owners = block_map[None, :] == jnp.arange(whole_dirs.shape[1])[:, None]
    perturb = jnp.einsum(
        "qb,be->qe", whole_dirs, owners.astype(jnp.float32), precision=lax.Precision.HIGHEST
    )
    forward_div = divergence(forward_state, coupling, inverse_size)
    adjoint_div = divergence(adjoint_state, coupling, inverse_size)

    def neighbour_fn(traces):
        from_south, from_north = rims_lat(traces[0], traces[1])
        from_west, from_east = rims_lon(traces[2], traces[3])
        sides = [from_south, from_north, from_west, from_east]
        horizontal = reorient(sides, face_codes, orient)
        below_trace, above_trace = radial_neighbours(traces[4], traces[5])
        return horizontal + [below_trace, above_trace]

    probe_count = inc_forward.shape[0]
    states = jnp.concatenate([inc_forward, inc_adjoint], 0)
    sources = pressure_source(perturb, forward_div, adjoint_div)
    updated = heun_step(
        states, sources, neighbour_fn, bulk_modulus, inverse_size, coupling, selects
    )
    new_forward = updated[:probe_count]
    new_adjoint = updated[probe_count:]
    element_terms = sensitivity(
        new_forward, new_adjoint, forward_div, adjoint_state, inverse_size, coupling, quadrature
    )
    partial_sums = jnp.einsum(
        "qe,be->qb", element_terms, owners.astype(jnp.float32), precision=lax.Precision.HIGHEST
    )
    hess_vec = scatter_sums(partial_sums)
    return (new_forward, new_adjoint, hess_vec)


def solution(mesh):
    placed = (
        P(None, ("lat", "lon")),
        P(None, ("lat", "lon")),
        P(None, None, ("lat", "lon")),
        P(None, None, ("lat", "lon")),
        P(("lat", "lon")),
        P(("lat", "lon")),
        P(None, ("lat", "lon")),
        P(("lat", "lon")),
        P(None, ("lat", "lon")),
    )
    return jax.shard_map(
        body,
        mesh=mesh,
        in_specs=placed,
        out_specs=(
            P(None, None, ("lat", "lon")),
            P(None, None, ("lat", "lon")),
            P(None, ("lat", "lon")),
        ),
        check_vma=False,
    )
```

```python
import jax
import jax.numpy as jnp
import numpy as np
from jax import lax
from jax.sharding import PartitionSpec as P

TIME_STEP = 0.05
PENALTY = 1.0
LIFT_FACTOR = 6.0


def shifted(block, axis, distance):
    devices = range(lax.axis_size(axis))
    route = [(i - distance, i) for i in devices if i - distance in devices]
    return lax.ppermute(block, axis, route)


def from_behind(value, axis, steps):
    count = lax.axis_size(axis)
    pairs = [(source, (source + steps) % count) for source in range(count)]
    return lax.ppermute(value, axis, pairs)


def node_tables():
    spread = 1.0 / np.sqrt(5.0)
    points = np.array([-1.0, -spread, spread, 1.0])
    weights = np.array([1.0, 5.0, 5.0, 1.0]) / 6.0
    products = np.array(
        [np.prod([points[j] - points[k] for k in range(4) if k != j]) for j in range(4)]
    )
    derivative = np.zeros((4, 4))
    for i in range(4):
        for j in range(4):
            if i != j:
                derivative[i, j] = products[i] / products[j] / (points[i] - points[j])
        derivative[i, i] = np.sum([1.0 / (points[i] - points[k]) for k in range(4) if k != i])
    identity = np.eye(4)
    directional = [
        np.kron(derivative, np.kron(identity, identity)),
        np.kron(identity, np.kron(derivative, identity)),
        np.kron(identity, np.kron(identity, derivative)),
    ]
    coupling = np.zeros((256, 256))
    for d in range(3):
        coupling[64 * (d + 1) : 64 * (d + 2), 0:64] = directional[d].T
        coupling[0:64, 64 * (d + 1) : 64 * (d + 2)] = directional[d].T
    selects = np.zeros((256, 192))
    for f in range(6):
        d = f // 2
        for u in range(4):
            for v in range(4):
                position = [u, v]
                position.insert(d, 3 * (f % 2))
                node_id = 16 * position[0] + 4 * position[1] + position[2]
                selects[node_id, 32 * f + 4 * u + v] = 1.0
                selects[64 * (d + 1) + node_id, 32 * f + 16 + 4 * u + v] = 1.0
    orient = np.zeros((8, 32), np.int32)
    for q in range(8):
        for u in range(4):
            for v in range(4):
                source_u, source_v = (v, u) if q & 1 else (u, v)
                if q & 2:
                    source_u = 3 - source_u
                if q & 4:
                    source_v = 3 - source_v
                orient[q, 4 * u + v] = 4 * source_u + source_v
                orient[q, 16 + 4 * u + v] = 16 + 4 * source_u + source_v
    quadrature = np.kron(weights, np.kron(weights, weights))
    return (
        jnp.asarray(coupling, dtype=jnp.float32),
        jnp.asarray(selects, dtype=jnp.float32),
        orient,
        jnp.asarray(quadrature, dtype=jnp.float32),
    )


def volume_rate(states, coupling, bulk_modulus, inverse_size, mixed=None):
    if mixed is None:
        mixed = jnp.einsum("cd,scr->sdr", coupling, states, precision=lax.Precision.HIGHEST)
    channel = lax.broadcasted_iota(jnp.int32, (256, 1), 0)
    factor = jnp.where(
        channel < 64, -(bulk_modulus * inverse_size)[None, :], -inverse_size[None, :]
    )
    return mixed * factor[None]


def face_term(own_trace, neighbour, bulk_modulus, inverse_size, normal_sign):
    jump_pressure = neighbour[:, :16] - own_trace[:, :16]
    jump_velocity = neighbour[:, 16:] - own_trace[:, 16:]
    modulus = bulk_modulus[None, None, :]
    lift_scale = LIFT_FACTOR * inverse_size[None, None, :]
    on_pressure = lift_scale * (
        -modulus * normal_sign * 0.5 * jump_velocity + 0.5 * PENALTY * jump_pressure
    )
    on_velocity = lift_scale * (-normal_sign * 0.5 * jump_pressure + 0.5 * PENALTY * jump_velocity)
    return jnp.concatenate([on_pressure, on_velocity], 1)


def radial_neighbours(rad_minus, rad_plus):
    below_trace = jnp.concatenate([jnp.zeros_like(rad_plus[..., :1]), rad_plus[..., :-1]], -1)
    above_trace = jnp.concatenate([rad_minus[..., 1:], jnp.zeros_like(rad_minus[..., :1])], -1)
    return (below_trace, above_trace)


def heun_step(
    states, sources, neighbour_fn, bulk_modulus, inverse_size, coupling, selects, mixed
):

    def rate_of(field_now, mixed=None):
        traces_all = jnp.einsum("ck,scr->skr", selects, field_now, precision=lax.Precision.HIGHEST)
        traces = [traces_all[:, 32 * f : 32 * f + 32] for f in range(6)]
        neighbours = neighbour_fn(traces)
        face_rates = jnp.concatenate(
            [
                face_term(traces[f], neighbours[f], bulk_modulus, inverse_size, 2.0 * (f % 2) - 1.0)
                for f in range(6)
            ],
            1,
        )
        lifted = jnp.einsum("ck,skr->scr", selects, face_rates, precision=lax.Precision.HIGHEST)
        volume = volume_rate(field_now, coupling, bulk_modulus, inverse_size, mixed)
        return volume + lifted + sources

    first_rate = rate_of(states, mixed)
    second_rate = rate_of(states + TIME_STEP * first_rate)
    return states + 0.5 * TIME_STEP * (first_rate + second_rate)


def divergence(field_state, coupling, inverse_size):
    return -inverse_size * jnp.einsum(
        "cn,...cr->...nr", coupling[:, :64], field_state, precision=lax.Precision.HIGHEST
    )


def pressure_source(perturb, forward_div, adjoint_div):
    source_terms = jnp.concatenate(
        [perturb[:, None, :] * forward_div[None], perturb[:, None, :] * adjoint_div[None]], 0
    )
    return jnp.concatenate(
        [source_terms, jnp.zeros((source_terms.shape[0], 192, source_terms.shape[2]), jnp.float32)],
        1,
    )


def sensitivity(
    new_forward, new_adjoint, forward_div, adjoint_state, inverse_size, coupling, quadrature
):
    new_div = divergence(new_forward, coupling, inverse_size)
    integrand = new_adjoint[:, :64] * forward_div[None] + adjoint_state[:64][None] * new_div
    return jnp.einsum("n,pnr->pr", quadrature, integrand, precision=lax.Precision.HIGHEST) / (
        64.0 * inverse_size**3
    )


def face_map(kind):
    picks = np.zeros((32, 32), np.float32)
    for part in range(2):
        for u in range(4):
            for v in range(4):
                su, sv = {"v": (u, 3 - v), "u": (3 - u, v), "t": (v, u)}[kind]
                picks[16 * part + 4 * u + v, 16 * part + 4 * su + sv] = 1.0
    return jnp.asarray(picks)


def reorient(sides, codes, orient):
    stacked = jnp.stack(sides, 0)
    for bit, kind in ((2, "v"), (1, "u"), (0, "t")):
        moved = jnp.einsum(
            "kj,fsjr->fskr", face_map(kind), stacked, precision=lax.Precision.HIGHEST
        )
        stacked = jnp.where(((codes & (1 << bit)) != 0)[:, None, None, :], moved, stacked)
    return [stacked[f] for f in range(len(sides))]


def gather_blocks(block):
    count = lax.axis_size(("lat", "lon"))
    spread = jnp.broadcast_to(block.T, (count, block.shape[0]))
    return lax.all_to_all(spread, ("lat", "lon"), 0, 0, tiled=True).T


def scatter_sums(partial):
    pieces = lax.all_to_all(partial.T, ("lat", "lon"), 0, 0, tiled=True)
    return jnp.sum(pieces, 0)[:, None]


def shift_lat(rim, offset):
    return shifted(rim, "lat", offset)


def shift_lon(rim, offset):
    return from_behind(rim, "lon", offset)


def rims_lat(first_rim, last_rim):
    from_south = shift_lat(last_rim, 1)
    from_north = shift_lat(first_rim, -1)
    return (from_south, from_north)


def rims_lon(first_rim, last_rim):
    from_west = shift_lon(last_rim, 1)
    from_east = shift_lon(first_rim, -1)
    return (from_west, from_east)


def body(
    forward_state,
    adjoint_state,
    inc_forward,
    inc_adjoint,
    bulk_modulus,
    inverse_size,
    face_codes,
    block_map,
    probe_dirs,
):
    coupling, selects, orient, quadrature = node_tables()
    whole_dirs = gather_blocks(probe_dirs)
    owners = block_map[None, :] == jnp.arange(whole_dirs.shape[1])[:, None]
    perturb = jnp.einsum(
        "qb,be->qe", whole_dirs, owners.astype(jnp.float32), precision=lax.Precision.HIGHEST
    )
    probe_count = inc_forward.shape[0]
    batch = jnp.concatenate(
        [inc_forward, inc_adjoint, forward_state[None], adjoint_state[None]], 0
    )
    mixed = jnp.einsum("cd,scr->sdr", coupling, batch, precision=lax.Precision.HIGHEST)
    forward_div = -inverse_size * mixed[2 * probe_count, :64]
    adjoint_div = -inverse_size * mixed[2 * probe_count + 1, :64]

    def neighbour_fn(traces):
        from_south, from_north = rims_lat(traces[0], traces[1])
        from_west, from_east = rims_lon(traces[2], traces[3])
        sides = [from_south, from_north, from_west, from_east]
        horizontal = reorient(sides, face_codes, orient)
        below_trace, above_trace = radial_neighbours(traces[4], traces[5])
        return horizontal + [below_trace, above_trace]

    states = batch[: 2 * probe_count]
    sources = pressure_source(perturb, forward_div, adjoint_div)
    updated = heun_step(
        states, sources, neighbour_fn, bulk_modulus, inverse_size, coupling, selects,
        mixed[: 2 * probe_count],
    )
    new_forward = updated[:probe_count]
    new_adjoint = updated[probe_count:]
    element_terms = sensitivity(
        new_forward, new_adjoint, forward_div, batch[2 * probe_count + 1], inverse_size,
        coupling, quadrature,
    )
    partial_sums = jnp.einsum(
        "qe,be->qb", element_terms, owners.astype(jnp.float32), precision=lax.Precision.HIGHEST
    )
    hess_vec = scatter_sums(partial_sums)
    return (new_forward, new_adjoint, hess_vec)


def solution(mesh):
    placed = (
        P(None, ("lat", "lon")),
        P(None, ("lat", "lon")),
        P(None, None, ("lat", "lon")),
        P(None, None, ("lat", "lon")),
        P(("lat", "lon")),
        P(("lat", "lon")),
        P(None, ("lat", "lon")),
        P(("lat", "lon")),
        P(None, ("lat", "lon")),
    )
    return jax.shard_map(
        body,
        mesh=mesh,
        in_specs=placed,
        out_specs=(
            P(None, None, ("lat", "lon")),
            P(None, None, ("lat", "lon")),
            P(None, ("lat", "lon")),
        ),
        check_vma=False,
    )
```

```python
import jax
import jax.numpy as jnp
import numpy as np
from jax import lax
from jax.sharding import PartitionSpec as P

TIME_STEP = 0.05
PENALTY = 1.0
LIFT_FACTOR = 6.0


def shifted(block, axis, distance):
    devices = range(lax.axis_size(axis))
    route = [(i - distance, i) for i in devices if i - distance in devices]
    return lax.ppermute(block, axis, route)


def from_behind(value, axis, steps):
    count = lax.axis_size(axis)
    pairs = [(source, (source + steps) % count) for source in range(count)]
    return lax.ppermute(value, axis, pairs)


def node_tables():
    spread = 1.0 / np.sqrt(5.0)
    points = np.array([-1.0, -spread, spread, 1.0])
    weights = np.array([1.0, 5.0, 5.0, 1.0]) / 6.0
    products = np.array(
        [np.prod([points[j] - points[k] for k in range(4) if k != j]) for j in range(4)]
    )
    derivative = np.zeros((4, 4))
    for i in range(4):
        for j in range(4):
            if i != j:
                derivative[i, j] = products[i] / products[j] / (points[i] - points[j])
        derivative[i, i] = np.sum([1.0 / (points[i] - points[k]) for k in range(4) if k != i])
    identity = np.eye(4)
    directional = [
        np.kron(derivative, np.kron(identity, identity)),
        np.kron(identity, np.kron(derivative, identity)),
        np.kron(identity, np.kron(identity, derivative)),
    ]
    coupling = np.zeros((256, 256))
    for d in range(3):
        coupling[64 * (d + 1) : 64 * (d + 2), 0:64] = directional[d].T
        coupling[0:64, 64 * (d + 1) : 64 * (d + 2)] = directional[d].T
    selects = np.zeros((256, 192))
    for f in range(6):
        d = f // 2
        for u in range(4):
            for v in range(4):
                position = [u, v]
                position.insert(d, 3 * (f % 2))
                node_id = 16 * position[0] + 4 * position[1] + position[2]
                selects[node_id, 32 * f + 4 * u + v] = 1.0
                selects[64 * (d + 1) + node_id, 32 * f + 16 + 4 * u + v] = 1.0
    orient = np.zeros((8, 32), np.int32)
    for q in range(8):
        for u in range(4):
            for v in range(4):
                source_u, source_v = (v, u) if q & 1 else (u, v)
                if q & 2:
                    source_u = 3 - source_u
                if q & 4:
                    source_v = 3 - source_v
                orient[q, 4 * u + v] = 4 * source_u + source_v
                orient[q, 16 + 4 * u + v] = 16 + 4 * source_u + source_v
    quadrature = np.kron(weights, np.kron(weights, weights))
    return (
        jnp.asarray(coupling, dtype=jnp.float32),
        jnp.asarray(selects, dtype=jnp.float32),
        orient,
        jnp.asarray(quadrature, dtype=jnp.float32),
    )


def volume_rate(states, coupling, bulk_modulus, inverse_size, mixed=None):
    if mixed is None:
        mixed = jnp.einsum("cd,scr->sdr", coupling, states, precision=lax.Precision.HIGHEST)
    channel = lax.broadcasted_iota(jnp.int32, (256, 1), 0)
    factor = jnp.where(
        channel < 64, -(bulk_modulus * inverse_size)[None, :], -inverse_size[None, :]
    )
    return mixed * factor[None]


def face_term(own_trace, neighbour, bulk_modulus, inverse_size, normal_sign):
    jump_pressure = neighbour[:, :16] - own_trace[:, :16]
    jump_velocity = neighbour[:, 16:] - own_trace[:, 16:]
    modulus = bulk_modulus[None, None, :]
    lift_scale = LIFT_FACTOR * inverse_size[None, None, :]
    on_pressure = lift_scale * (
        -modulus * normal_sign * 0.5 * jump_velocity + 0.5 * PENALTY * jump_pressure
    )
    on_velocity = lift_scale * (-normal_sign * 0.5 * jump_pressure + 0.5 * PENALTY * jump_velocity)
    return jnp.concatenate([on_pressure, on_velocity], 1)


def radial_neighbours(rad_minus, rad_plus):
    below_trace = jnp.concatenate([jnp.zeros_like(rad_plus[..., :1]), rad_plus[..., :-1]], -1)
    above_trace = jnp.concatenate([rad_minus[..., 1:], jnp.zeros_like(rad_minus[..., :1])], -1)
    return (below_trace, above_trace)


def heun_step(
    states, sources, neighbour_fn, bulk_modulus, inverse_size, coupling, selects, mixed
):

    def rate_of(field_now, mixed=None):
        traces_all = jnp.einsum("ck,scr->skr", selects, field_now, precision=lax.Precision.HIGHEST)
        traces = [traces_all[:, 32 * f : 32 * f + 32] for f in range(6)]
        neighbours = neighbour_fn(traces)
        face_rates = jnp.concatenate(
            [
                face_term(traces[f], neighbours[f], bulk_modulus, inverse_size, 2.0 * (f % 2) - 1.0)
                for f in range(6)
            ],
            1,
        )
        lifted = jnp.einsum("ck,skr->scr", selects, face_rates, precision=lax.Precision.HIGHEST)
        volume = volume_rate(field_now, coupling, bulk_modulus, inverse_size, mixed)
        return volume + lifted + sources

    first_rate = rate_of(states, mixed)
    second_rate = rate_of(states + TIME_STEP * first_rate)
    return states + 0.5 * TIME_STEP * (first_rate + second_rate)


def divergence(field_state, coupling, inverse_size):
    return -inverse_size * jnp.einsum(
        "cn,...cr->...nr", coupling[:, :64], field_state, precision=lax.Precision.HIGHEST
    )


def pressure_source(perturb, forward_div, adjoint_div):
    source_terms = jnp.concatenate(
        [perturb[:, None, :] * forward_div[None], perturb[:, None, :] * adjoint_div[None]], 0
    )
    return jnp.concatenate(
        [source_terms, jnp.zeros((source_terms.shape[0], 192, source_terms.shape[2]), jnp.float32)],
        1,
    )


def sensitivity(
    new_forward, new_adjoint, forward_div, adjoint_state, inverse_size, coupling, quadrature
):
    own = jnp.einsum(
        "n,pnr->pr", quadrature, new_adjoint[:, :64] * forward_div[None],
        precision=lax.Precision.HIGHEST,
    )
    weighted = coupling[:, :64] * quadrature[None, :]
    pulled = jnp.einsum(
        "cn,nr->cr", weighted, adjoint_state[:64], precision=lax.Precision.HIGHEST
    )
    crossed = jnp.einsum("pcr,cr->pr", new_forward, pulled, precision=lax.Precision.HIGHEST)
    return (own - inverse_size * crossed) / (64.0 * inverse_size**3)


def face_map(kind):
    picks = np.zeros((32, 32), np.float32)
    for part in range(2):
        for u in range(4):
            for v in range(4):
                su, sv = {"v": (u, 3 - v), "u": (3 - u, v), "t": (v, u)}[kind]
                picks[16 * part + 4 * u + v, 16 * part + 4 * su + sv] = 1.0
    return jnp.asarray(picks)


def reorient(sides, codes, orient):
    stacked = jnp.stack(sides, 0)
    for bit, kind in ((2, "v"), (1, "u"), (0, "t")):
        moved = jnp.einsum(
            "kj,fsjr->fskr", face_map(kind), stacked, precision=lax.Precision.HIGHEST
        )
        stacked = jnp.where(((codes & (1 << bit)) != 0)[:, None, None, :], moved, stacked)
    return [stacked[f] for f in range(len(sides))]


def gather_blocks(block):
    count = lax.axis_size(("lat", "lon"))
    spread = jnp.broadcast_to(block.T, (count, block.shape[0]))
    return lax.all_to_all(spread, ("lat", "lon"), 0, 0, tiled=True).T


def scatter_sums(partial):
    pieces = lax.all_to_all(partial.T, ("lat", "lon"), 0, 0, tiled=True)
    return jnp.sum(pieces, 0)[:, None]


def shift_lat(rim, offset):
    return shifted(rim, "lat", offset)


def shift_lon(rim, offset):
    return from_behind(rim, "lon", offset)


def rims_lat(first_rim, last_rim):
    from_south = shift_lat(last_rim, 1)
    from_north = shift_lat(first_rim, -1)
    return (from_south, from_north)


def rims_lon(first_rim, last_rim):
    from_west = shift_lon(last_rim, 1)
    from_east = shift_lon(first_rim, -1)
    return (from_west, from_east)


def body(
    forward_state,
    adjoint_state,
    inc_forward,
    inc_adjoint,
    bulk_modulus,
    inverse_size,
    face_codes,
    block_map,
    probe_dirs,
):
    coupling, selects, orient, quadrature = node_tables()
    whole_dirs = gather_blocks(probe_dirs)
    owners = block_map[None, :] == jnp.arange(whole_dirs.shape[1])[:, None]
    perturb = jnp.einsum(
        "qb,be->qe", whole_dirs, owners.astype(jnp.float32), precision=lax.Precision.HIGHEST
    )
    probe_count = inc_forward.shape[0]
    batch = jnp.concatenate(
        [inc_forward, inc_adjoint, forward_state[None], adjoint_state[None]], 0
    )
    mixed = jnp.einsum("cd,scr->sdr", coupling, batch, precision=lax.Precision.HIGHEST)
    forward_div = -inverse_size * mixed[2 * probe_count, :64]
    adjoint_div = -inverse_size * mixed[2 * probe_count + 1, :64]

    def neighbour_fn(traces):
        from_south, from_north = rims_lat(traces[0], traces[1])
        from_west, from_east = rims_lon(traces[2], traces[3])
        sides = [from_south, from_north, from_west, from_east]
        horizontal = reorient(sides, face_codes, orient)
        below_trace, above_trace = radial_neighbours(traces[4], traces[5])
        return horizontal + [below_trace, above_trace]

    states = batch[: 2 * probe_count]
    sources = pressure_source(perturb, forward_div, adjoint_div)
    updated = heun_step(
        states, sources, neighbour_fn, bulk_modulus, inverse_size, coupling, selects,
        mixed[: 2 * probe_count],
    )
    new_forward = updated[:probe_count]
    new_adjoint = updated[probe_count:]
    element_terms = sensitivity(
        new_forward, new_adjoint, forward_div, adjoint_state, inverse_size, coupling, quadrature
    )
    partial_sums = jnp.einsum(
        "qe,be->qb", element_terms, owners.astype(jnp.float32), precision=lax.Precision.HIGHEST
    )
    hess_vec = scatter_sums(partial_sums)
    return (new_forward, new_adjoint, hess_vec)


def solution(mesh):
    placed = (
        P(None, ("lat", "lon")),
        P(None, ("lat", "lon")),
        P(None, None, ("lat", "lon")),
        P(None, None, ("lat", "lon")),
        P(("lat", "lon")),
        P(("lat", "lon")),
        P(None, ("lat", "lon")),
        P(("lat", "lon")),
        P(None, ("lat", "lon")),
    )
    return jax.shard_map(
        body,
        mesh=mesh,
        in_specs=placed,
        out_specs=(
            P(None, None, ("lat", "lon")),
            P(None, None, ("lat", "lon")),
            P(None, ("lat", "lon")),
        ),
        check_vma=False,
    )
```

```python
import jax
import jax.numpy as jnp
import numpy as np
from jax import lax
from jax.sharding import PartitionSpec as P

TIME_STEP = 0.05
PENALTY = 1.0
LIFT_FACTOR = 6.0


def shifted(block, axis, distance):
    devices = range(lax.axis_size(axis))
    route = [(i - distance, i) for i in devices if i - distance in devices]
    return lax.ppermute(block, axis, route)


def from_behind(value, axis, steps):
    count = lax.axis_size(axis)
    pairs = [(source, (source + steps) % count) for source in range(count)]
    return lax.ppermute(value, axis, pairs)


def node_tables():
    spread = 1.0 / np.sqrt(5.0)
    points = np.array([-1.0, -spread, spread, 1.0])
    weights = np.array([1.0, 5.0, 5.0, 1.0]) / 6.0
    products = np.array(
        [np.prod([points[j] - points[k] for k in range(4) if k != j]) for j in range(4)]
    )
    derivative = np.zeros((4, 4))
    for i in range(4):
        for j in range(4):
            if i != j:
                derivative[i, j] = products[i] / products[j] / (points[i] - points[j])
        derivative[i, i] = np.sum([1.0 / (points[i] - points[k]) for k in range(4) if k != i])
    identity = np.eye(4)
    directional = [
        np.kron(derivative, np.kron(identity, identity)),
        np.kron(identity, np.kron(derivative, identity)),
        np.kron(identity, np.kron(identity, derivative)),
    ]
    coupling = np.zeros((256, 256))
    for d in range(3):
        coupling[64 * (d + 1) : 64 * (d + 2), 0:64] = directional[d].T
        coupling[0:64, 64 * (d + 1) : 64 * (d + 2)] = directional[d].T
    selects = np.zeros((256, 192))
    for f in range(6):
        d = f // 2
        for u in range(4):
            for v in range(4):
                position = [u, v]
                position.insert(d, 3 * (f % 2))
                node_id = 16 * position[0] + 4 * position[1] + position[2]
                selects[node_id, 32 * f + 4 * u + v] = 1.0
                selects[64 * (d + 1) + node_id, 32 * f + 16 + 4 * u + v] = 1.0
    orient = np.zeros((8, 32), np.int32)
    for q in range(8):
        for u in range(4):
            for v in range(4):
                source_u, source_v = (v, u) if q & 1 else (u, v)
                if q & 2:
                    source_u = 3 - source_u
                if q & 4:
                    source_v = 3 - source_v
                orient[q, 4 * u + v] = 4 * source_u + source_v
                orient[q, 16 + 4 * u + v] = 16 + 4 * source_u + source_v
    quadrature = np.kron(weights, np.kron(weights, weights))
    return (
        jnp.asarray(coupling, dtype=jnp.float32),
        jnp.asarray(selects, dtype=jnp.float32),
        orient,
        jnp.asarray(quadrature, dtype=jnp.float32),
    )


def volume_rate(states, coupling, bulk_modulus, inverse_size, mixed=None):
    if mixed is None:
        mixed = jnp.einsum("cd,scr->sdr", coupling, states, precision=lax.Precision.HIGHEST)
    channel = lax.broadcasted_iota(jnp.int32, (256, 1), 0)
    factor = jnp.where(
        channel < 64, -(bulk_modulus * inverse_size)[None, :], -inverse_size[None, :]
    )
    return mixed * factor[None]


def face_term(own_trace, neighbour, bulk_modulus, inverse_size, normal_sign):
    jump_pressure = neighbour[:, :16] - own_trace[:, :16]
    jump_velocity = neighbour[:, 16:] - own_trace[:, 16:]
    modulus = bulk_modulus[None, None, :]
    lift_scale = LIFT_FACTOR * inverse_size[None, None, :]
    on_pressure = lift_scale * (
        -modulus * normal_sign * 0.5 * jump_velocity + 0.5 * PENALTY * jump_pressure
    )
    on_velocity = lift_scale * (-normal_sign * 0.5 * jump_pressure + 0.5 * PENALTY * jump_velocity)
    return jnp.concatenate([on_pressure, on_velocity], 1)


def radial_neighbours(rad_minus, rad_plus):
    below_trace = jnp.concatenate([jnp.zeros_like(rad_plus[..., :1]), rad_plus[..., :-1]], -1)
    above_trace = jnp.concatenate([rad_minus[..., 1:], jnp.zeros_like(rad_minus[..., :1])], -1)
    return (below_trace, above_trace)


def heun_step(
    states, sources, neighbour_fn, bulk_modulus, inverse_size, coupling, selects, mixed
):

    def rate_of(field_now, mixed=None):
        traces_all = jnp.einsum("ck,scr->skr", selects, field_now, precision=lax.Precision.HIGHEST)
        traces = [traces_all[:, 32 * f : 32 * f + 32] for f in range(6)]
        neighbours = neighbour_fn(traces)
        face_rates = jnp.concatenate(
            [
                face_term(traces[f], neighbours[f], bulk_modulus, inverse_size, 2.0 * (f % 2) - 1.0)
                for f in range(6)
            ],
            1,
        )
        lifted = jnp.einsum("ck,skr->scr", selects, face_rates, precision=lax.Precision.HIGHEST)
        if mixed is None:
            field_now, _ = lax.optimization_barrier((field_now, neighbours[6]))
        volume = volume_rate(field_now, coupling, bulk_modulus, inverse_size, mixed)
        return volume + lifted + sources

    first_rate = rate_of(states, mixed)
    second_rate = rate_of(states + TIME_STEP * first_rate)
    return states + 0.5 * TIME_STEP * (first_rate + second_rate)


def divergence(field_state, coupling, inverse_size):
    return -inverse_size * jnp.einsum(
        "cn,...cr->...nr", coupling[:, :64], field_state, precision=lax.Precision.HIGHEST
    )


def pressure_source(perturb, forward_div, adjoint_div):
    source_terms = jnp.concatenate(
        [perturb[:, None, :] * forward_div[None], perturb[:, None, :] * adjoint_div[None]], 0
    )
    return jnp.concatenate(
        [source_terms, jnp.zeros((source_terms.shape[0], 192, source_terms.shape[2]), jnp.float32)],
        1,
    )


def sensitivity(
    new_forward, new_adjoint, forward_div, adjoint_state, inverse_size, coupling, quadrature
):
    own = jnp.einsum(
        "n,pnr->pr", quadrature, new_adjoint[:, :64] * forward_div[None],
        precision=lax.Precision.HIGHEST,
    )
    weighted = coupling[:, :64] * quadrature[None, :]
    pulled = jnp.einsum(
        "cn,nr->cr", weighted, adjoint_state[:64], precision=lax.Precision.HIGHEST
    )
    crossed = jnp.einsum("pcr,cr->pr", new_forward, pulled, precision=lax.Precision.HIGHEST)
    return (own - inverse_size * crossed) / (64.0 * inverse_size**3)


def face_map(kind):
    picks = np.zeros((32, 32), np.float32)
    for part in range(2):
        for u in range(4):
            for v in range(4):
                su, sv = {"v": (u, 3 - v), "u": (3 - u, v), "t": (v, u)}[kind]
                picks[16 * part + 4 * u + v, 16 * part + 4 * su + sv] = 1.0
    return jnp.asarray(picks)


def reorient(sides, codes, orient):
    stacked = jnp.stack(sides, 0)
    for bit, kind in ((2, "v"), (1, "u"), (0, "t")):
        moved = jnp.einsum(
            "kj,fsjr->fskr", face_map(kind), stacked, precision=lax.Precision.HIGHEST
        )
        stacked = jnp.where(((codes & (1 << bit)) != 0)[:, None, None, :], moved, stacked)
    return [stacked[f] for f in range(len(sides))]


def gather_blocks(block):
    count = lax.axis_size(("lat", "lon"))
    spread = jnp.broadcast_to(block.T, (count, block.shape[0]))
    return lax.all_to_all(spread, ("lat", "lon"), 0, 0, tiled=True).T


def scatter_sums(partial):
    pieces = lax.all_to_all(partial.T, ("lat", "lon"), 0, 0, tiled=True)
    return jnp.sum(pieces, 0)[:, None]


def shift_lat(rim, offset):
    return shifted(rim, "lat", offset)


def shift_lon(rim, offset):
    return from_behind(rim, "lon", offset)


def rims_lat(first_rim, last_rim):
    from_south = shift_lat(last_rim, 1)
    from_north = shift_lat(first_rim, -1)
    return (from_south, from_north)


def rims_lon(first_rim, last_rim):
    from_west = shift_lon(last_rim, 1)
    from_east = shift_lon(first_rim, -1)
    return (from_west, from_east)


def body(
    forward_state,
    adjoint_state,
    inc_forward,
    inc_adjoint,
    bulk_modulus,
    inverse_size,
    face_codes,
    block_map,
    probe_dirs,
):
    coupling, selects, orient, quadrature = node_tables()
    whole_dirs = gather_blocks(probe_dirs)
    owners = block_map[None, :] == jnp.arange(whole_dirs.shape[1])[:, None]
    perturb = jnp.einsum(
        "qb,be->qe", whole_dirs, owners.astype(jnp.float32), precision=lax.Precision.HIGHEST
    )
    probe_count = inc_forward.shape[0]
    batch = jnp.concatenate(
        [inc_forward, inc_adjoint, forward_state[None], adjoint_state[None]], 0
    )
    mixed = jnp.einsum("cd,scr->sdr", coupling, batch, precision=lax.Precision.HIGHEST)
    forward_div = -inverse_size * mixed[2 * probe_count, :64]
    adjoint_div = -inverse_size * mixed[2 * probe_count + 1, :64]

    def neighbour_fn(traces):
        from_south, from_north = rims_lat(traces[0], traces[1])
        from_west, from_east = rims_lon(traces[2], traces[3])
        sides = [from_south, from_north, from_west, from_east]
        horizontal = reorient(sides, face_codes, orient)
        below_trace, above_trace = radial_neighbours(traces[4], traces[5])
        return horizontal + [below_trace, above_trace, from_south]

    states = batch[: 2 * probe_count]
    sources = pressure_source(perturb, forward_div, adjoint_div)
    updated = heun_step(
        states, sources, neighbour_fn, bulk_modulus, inverse_size, coupling, selects,
        mixed[: 2 * probe_count],
    )
    new_forward = updated[:probe_count]
    new_adjoint = updated[probe_count:]
    element_terms = sensitivity(
        new_forward, new_adjoint, forward_div, adjoint_state, inverse_size, coupling, quadrature
    )
    partial_sums = jnp.einsum(
        "qe,be->qb", element_terms, owners.astype(jnp.float32), precision=lax.Precision.HIGHEST
    )
    hess_vec = scatter_sums(partial_sums)
    return (new_forward, new_adjoint, hess_vec)


def solution(mesh):
    placed = (
        P(None, ("lat", "lon")),
        P(None, ("lat", "lon")),
        P(None, None, ("lat", "lon")),
        P(None, None, ("lat", "lon")),
        P(("lat", "lon")),
        P(("lat", "lon")),
        P(None, ("lat", "lon")),
        P(("lat", "lon")),
        P(None, ("lat", "lon")),
    )
    return jax.shard_map(
        body,
        mesh=mesh,
        in_specs=placed,
        out_specs=(
            P(None, None, ("lat", "lon")),
            P(None, None, ("lat", "lon")),
            P(None, ("lat", "lon")),
        ),
        check_vma=False,
    )
```

```python
import jax
import jax.numpy as jnp
import numpy as np
from jax import lax
from jax.sharding import PartitionSpec as P
from jax.experimental.layout import Layout, with_layout_constraint

TIME_STEP = 0.05
PENALTY = 1.0
LIFT_FACTOR = 6.0


def shifted(block, axis, distance):
    devices = range(lax.axis_size(axis))
    route = [(i - distance, i) for i in devices if i - distance in devices]
    return lax.ppermute(block, axis, route)


def from_behind(value, axis, steps):
    count = lax.axis_size(axis)
    pairs = [(source, (source + steps) % count) for source in range(count)]
    return lax.ppermute(value, axis, pairs)


def node_tables():
    spread = 1.0 / np.sqrt(5.0)
    points = np.array([-1.0, -spread, spread, 1.0])
    weights = np.array([1.0, 5.0, 5.0, 1.0]) / 6.0
    products = np.array(
        [np.prod([points[j] - points[k] for k in range(4) if k != j]) for j in range(4)]
    )
    derivative = np.zeros((4, 4))
    for i in range(4):
        for j in range(4):
            if i != j:
                derivative[i, j] = products[i] / products[j] / (points[i] - points[j])
        derivative[i, i] = np.sum([1.0 / (points[i] - points[k]) for k in range(4) if k != i])
    identity = np.eye(4)
    directional = [
        np.kron(derivative, np.kron(identity, identity)),
        np.kron(identity, np.kron(derivative, identity)),
        np.kron(identity, np.kron(identity, derivative)),
    ]
    coupling = np.zeros((256, 256))
    for d in range(3):
        coupling[64 * (d + 1) : 64 * (d + 2), 0:64] = directional[d].T
        coupling[0:64, 64 * (d + 1) : 64 * (d + 2)] = directional[d].T
    selects = np.zeros((256, 192))
    for f in range(6):
        d = f // 2
        for u in range(4):
            for v in range(4):
                position = [u, v]
                position.insert(d, 3 * (f % 2))
                node_id = 16 * position[0] + 4 * position[1] + position[2]
                selects[node_id, 32 * f + 4 * u + v] = 1.0
                selects[64 * (d + 1) + node_id, 32 * f + 16 + 4 * u + v] = 1.0
    orient = np.zeros((8, 32), np.int32)
    for q in range(8):
        for u in range(4):
            for v in range(4):
                source_u, source_v = (v, u) if q & 1 else (u, v)
                if q & 2:
                    source_u = 3 - source_u
                if q & 4:
                    source_v = 3 - source_v
                orient[q, 4 * u + v] = 4 * source_u + source_v
                orient[q, 16 + 4 * u + v] = 16 + 4 * source_u + source_v
    quadrature = np.kron(weights, np.kron(weights, weights))
    return (
        jnp.asarray(coupling, dtype=jnp.float32),
        jnp.asarray(selects, dtype=jnp.float32),
        orient,
        jnp.asarray(quadrature, dtype=jnp.float32),
    )


def volume_rate(states, coupling, bulk_modulus, inverse_size, mixed=None):
    if mixed is None:
        mixed = jnp.einsum("cd,scr->sdr", coupling, states, precision=lax.Precision.HIGHEST)
    channel = lax.broadcasted_iota(jnp.int32, (256, 1), 0)
    factor = jnp.where(
        channel < 64, -(bulk_modulus * inverse_size)[None, :], -inverse_size[None, :]
    )
    return mixed * factor[None]


def face_term(own_trace, neighbour, bulk_modulus, inverse_size, normal_sign):
    jump_pressure = neighbour[:, :16] - own_trace[:, :16]
    jump_velocity = neighbour[:, 16:] - own_trace[:, 16:]
    modulus = bulk_modulus[None, None, :]
    lift_scale = LIFT_FACTOR * inverse_size[None, None, :]
    on_pressure = lift_scale * (
        -modulus * normal_sign * 0.5 * jump_velocity + 0.5 * PENALTY * jump_pressure
    )
    on_velocity = lift_scale * (-normal_sign * 0.5 * jump_pressure + 0.5 * PENALTY * jump_velocity)
    return jnp.concatenate([on_pressure, on_velocity], 1)


def radial_neighbours(rad_minus, rad_plus):
    below_trace = jnp.concatenate([jnp.zeros_like(rad_plus[..., :1]), rad_plus[..., :-1]], -1)
    above_trace = jnp.concatenate([rad_minus[..., 1:], jnp.zeros_like(rad_minus[..., :1])], -1)
    return (below_trace, above_trace)


def heun_step(
    states, sources, neighbour_fn, bulk_modulus, inverse_size, coupling, selects, mixed
):

    def rate_of(field_now, mixed=None):
        traces_all = jnp.einsum("ck,scr->skr", selects, field_now, precision=lax.Precision.HIGHEST)
        traces = [traces_all[:, 32 * f : 32 * f + 32] for f in range(6)]
        neighbours = neighbour_fn(traces)
        face_rates = jnp.concatenate(
            [
                face_term(traces[f], neighbours[f], bulk_modulus, inverse_size, 2.0 * (f % 2) - 1.0)
                for f in range(6)
            ],
            1,
        )
        lifted = jnp.einsum("ck,skr->scr", selects, face_rates, precision=lax.Precision.HIGHEST)
        volume = volume_rate(field_now, coupling, bulk_modulus, inverse_size, mixed)
        return volume + lifted + sources

    first_rate = rate_of(states, mixed)
    second_rate = rate_of(states + TIME_STEP * first_rate)
    return states + 0.5 * TIME_STEP * (first_rate + second_rate)


def divergence(field_state, coupling, inverse_size):
    return -inverse_size * jnp.einsum(
        "cn,...cr->...nr", coupling[:, :64], field_state, precision=lax.Precision.HIGHEST
    )


def pressure_source(perturb, forward_div, adjoint_div):
    source_terms = jnp.concatenate(
        [perturb[:, None, :] * forward_div[None], perturb[:, None, :] * adjoint_div[None]], 0
    )
    return jnp.concatenate(
        [source_terms, jnp.zeros((source_terms.shape[0], 192, source_terms.shape[2]), jnp.float32)],
        1,
    )


def sensitivity(
    new_forward, new_adjoint, forward_div, adjoint_state, inverse_size, coupling, quadrature
):
    own = jnp.einsum(
        "n,pnr->pr", quadrature, new_adjoint[:, :64] * forward_div[None],
        precision=lax.Precision.HIGHEST,
    )
    weighted = coupling[:, :64] * quadrature[None, :]
    pulled = jnp.einsum(
        "cn,nr->cr", weighted, adjoint_state[:64], precision=lax.Precision.HIGHEST
    )
    crossed = jnp.einsum("pcr,cr->pr", new_forward, pulled, precision=lax.Precision.HIGHEST)
    return (own - inverse_size * crossed) / (64.0 * inverse_size**3)


def face_map(kind):
    picks = np.zeros((32, 32), np.float32)
    for part in range(2):
        for u in range(4):
            for v in range(4):
                su, sv = {"v": (u, 3 - v), "u": (3 - u, v), "t": (v, u)}[kind]
                picks[16 * part + 4 * u + v, 16 * part + 4 * su + sv] = 1.0
    return jnp.asarray(picks)


def reorient(sides, codes, orient):
    stacked = jnp.stack(sides, 0)
    for bit, kind in ((2, "v"), (1, "u"), (0, "t")):
        moved = jnp.einsum(
            "kj,fsjr->fskr", face_map(kind), stacked, precision=lax.Precision.HIGHEST
        )
        stacked = jnp.where(((codes & (1 << bit)) != 0)[:, None, None, :], moved, stacked)
    return [stacked[f] for f in range(len(sides))]


def gather_blocks(block):
    count = lax.axis_size(("lat", "lon"))
    spread = jnp.broadcast_to(block.T, (count, block.shape[0]))
    return lax.all_to_all(spread, ("lat", "lon"), 0, 0, tiled=True).T


def scatter_sums(partial):
    pieces = lax.all_to_all(partial.T, ("lat", "lon"), 0, 0, tiled=True)
    return jnp.sum(pieces, 0)[:, None]


def shift_lat(rim, offset):
    return shifted(rim, "lat", offset)


def shift_lon(rim, offset):
    return from_behind(rim, "lon", offset)


def rims_lat(first_rim, last_rim):
    from_south = shift_lat(last_rim, 1)
    from_north = shift_lat(first_rim, -1)
    return (from_south, from_north)


def rims_lon(first_rim, last_rim):
    from_west = shift_lon(last_rim, 1)
    from_east = shift_lon(first_rim, -1)
    return (from_west, from_east)


def body(
    forward_state,
    adjoint_state,
    inc_forward,
    inc_adjoint,
    bulk_modulus,
    inverse_size,
    face_codes,
    block_map,
    probe_dirs,
):
    coupling, selects, orient, quadrature = node_tables()
    whole_dirs = gather_blocks(probe_dirs)
    owners = block_map[None, :] == jnp.arange(whole_dirs.shape[1])[:, None]
    perturb = jnp.einsum(
        "qb,be->qe", whole_dirs, owners.astype(jnp.float32), precision=lax.Precision.HIGHEST
    )
    probe_count = inc_forward.shape[0]
    batch = jnp.concatenate(
        [inc_forward, inc_adjoint, forward_state[None], adjoint_state[None]], 0
    )
    batch = with_layout_constraint(batch, Layout(major_to_minor=(0, 1, 2)))
    mixed = jnp.einsum("cd,scr->sdr", coupling, batch, precision=lax.Precision.HIGHEST)
    forward_div = -inverse_size * mixed[2 * probe_count, :64]
    adjoint_div = -inverse_size * mixed[2 * probe_count + 1, :64]

    def neighbour_fn(traces):
        from_south, from_north = rims_lat(traces[0], traces[1])
        from_west, from_east = rims_lon(traces[2], traces[3])
        sides = [from_south, from_north, from_west, from_east]
        horizontal = reorient(sides, face_codes, orient)
        below_trace, above_trace = radial_neighbours(traces[4], traces[5])
        return horizontal + [below_trace, above_trace]

    states = batch[: 2 * probe_count]
    sources = pressure_source(perturb, forward_div, adjoint_div)
    updated = heun_step(
        states, sources, neighbour_fn, bulk_modulus, inverse_size, coupling, selects,
        mixed[: 2 * probe_count],
    )
    new_forward = updated[:probe_count]
    new_adjoint = updated[probe_count:]
    element_terms = sensitivity(
        new_forward, new_adjoint, forward_div, adjoint_state, inverse_size, coupling, quadrature
    )
    partial_sums = jnp.einsum(
        "qe,be->qb", element_terms, owners.astype(jnp.float32), precision=lax.Precision.HIGHEST
    )
    hess_vec = scatter_sums(partial_sums)
    return (new_forward, new_adjoint, hess_vec)


def solution(mesh):
    placed = (
        P(None, ("lat", "lon")),
        P(None, ("lat", "lon")),
        P(None, None, ("lat", "lon")),
        P(None, None, ("lat", "lon")),
        P(("lat", "lon")),
        P(("lat", "lon")),
        P(None, ("lat", "lon")),
        P(("lat", "lon")),
        P(None, ("lat", "lon")),
    )
    return jax.shard_map(
        body,
        mesh=mesh,
        in_specs=placed,
        out_specs=(
            P(None, None, ("lat", "lon")),
            P(None, None, ("lat", "lon")),
            P(None, ("lat", "lon")),
        ),
        check_vma=False,
    )
```
